32 devices in a mesh: blk: 8 (over z, y), dp: 4 (over x, core).
Axes of the slice: x: 2, y: 2, z: 4, core: 2. Of those that a mesh axis runs over, the one named last changes fastest.
Arguments:
- feature_map: bfloat16 [20480, 320], P(('blk', 'dp')), may hold values from -8 to 8, as said below
- head_weight: bfloat16 [320, 1280], replicated, may hold values from -0.3125 to 0.3125
- head_shift: float32 [1280], replicated, may hold values from -0.5 to 0.5
- proj_weight: bfloat16 [1280, 256], replicated, may hold values from -0.15625 to 0.15625
Outputs:
- loss: float32 [], replicated
- grad_head: float32 [320, 1280], replicated
- grad_shift: float32 [1280], replicated
- grad_proj: float32 [1280, 256], replicated
The draws below stay inside these ranges and needn't reach their ends.
Inputs may be any that keep to these rules, and one draw needn't show every extreme that they name: `feature_map`: features of order one.
All inputs are finite; a program needn't handle non-finite values.
Results may differ from the reference program's by a relative error of at most 0.00067.
Values may be sent and summed in bfloat16 or wider, within the bound.
No kernel may reach another device: no remote copies, remote signals or barrier semaphores. Data moves between devices by JAX's collectives and lax.ppermute only.
A program may use at most 64 MiB of HBM per device.

```python
import math
import jax
import jax.numpy as jnp
from jax import lax

C_IN = 320
C_HEAD = 1280
PROJ = 256
POS = 16
BATCH = 1280


def draw_feature_map(key, part):
    key_class = jax.random.fold_in(key, 11)
    key_center = jax.random.fold_in(key, 12)
    key_image = jax.random.fold_in(key, 13)
    key_noise = jax.random.fold_in(key, 14)
    classes = jax.random.randint(key_class, (BATCH,), 0, 8)
    centers = jax.random.normal(key_center, (8, C_IN), jnp.float32)
    own = jax.random.normal(key_image, (BATCH, C_IN), jnp.float32)
    noise = jax.random.normal(key_noise, (BATCH, POS, C_IN), jnp.float32)
    shared = 1.2 * centers[classes] + 0.8 * own
    rows = shared[:, None, :] + 0.6 * noise
    rows = jnp.clip(rows, -8.0, 8.0)
    return rows.reshape(BATCH * POS, C_IN).astype(jnp.bfloat16)


def scatter_about(stream_key, dims, width, bound, kind=jnp.bfloat16):
    return jnp.clip(width * jax.random.normal(stream_key, dims, jnp.float32), -bound, bound).astype(kind)


def setup_inputs(seed: int = 0) -> dict:
    arg_keys = jax.random.split(jax.random.key(seed), 5)
    feature_map = draw_feature_map(jax.random.fold_in(arg_keys[4], 71), 0)
    head_weight = scatter_about(arg_keys[1], (C_IN, C_HEAD), C_IN ** -0.5, 0.3125)
    head_shift = jnp.clip(jax.random.uniform(arg_keys[2], (C_HEAD,), jnp.float32, -0.5, 0.5), -0.5, 0.5)
    proj_weight = scatter_about(arg_keys[3], (C_HEAD, PROJ), C_HEAD ** -0.5, 0.15625)
    return dict(feature_map=feature_map, head_weight=head_weight, head_shift=head_shift, proj_weight=proj_weight)


def reference(feature_map, head_weight, head_shift, proj_weight):
    pre = jnp.dot(feature_map, head_weight, preferred_element_type=jnp.float32) + head_shift
    act = jax.nn.silu(pre)
    pooled = lax.optimization_barrier(jnp.mean(act.reshape(BATCH, POS, C_HEAD), axis=1)).astype(jnp.bfloat16)
    proj = jnp.dot(pooled, proj_weight, preferred_element_type=jnp.float32)
    rnorm = jnp.sqrt(lax.optimization_barrier(jnp.sum(proj * proj, axis=1, keepdims=True)) + 1e-06)
    unit = proj / rnorm
    zed = unit.astype(jnp.bfloat16)
    block = math.gcd(BATCH, 512)
    count = BATCH // block

    def one_block(index):
        start = index * block
        rows_z = lax.dynamic_slice_in_dim(zed, start, block, 0)
        sim = lax.dot_general(rows_z, zed, (((1,), (1,)), ((), ())), preferred_element_type=jnp.float32)
        kern = jnp.exp(4.0 * (sim - 1.0))
        row_ids = start + jnp.arange(block, dtype=jnp.int32)
        col_ids = jnp.arange(BATCH, dtype=jnp.int32)
        kern = jnp.where(row_ids[:, None] == col_ids[None, :], jnp.float32(0.0), kern)
        srow = lax.optimization_barrier(jnp.sum(kern, axis=1))
        numer = jnp.dot(kern.astype(jnp.bfloat16), zed, preferred_element_type=jnp.float32)
        return (srow, numer)
    srow, numer = lax.map(one_block, jnp.arange(count, dtype=jnp.int32))
    srow = srow.reshape(BATCH)
    numer = numer.reshape(BATCH, PROJ)
    total = jnp.sum(srow)
    loss = jnp.log(total / (BATCH * (BATCH - 1.0)))
    grad_unit = BATCH * 8.0 / total * numer
    grad_rows = ((grad_unit - unit * lax.optimization_barrier(jnp.sum(unit * grad_unit, axis=1, keepdims=True))) / rnorm).astype(jnp.bfloat16)
    grad_proj = lax.dot_general(pooled, grad_rows, (((0,), (0,)), ((), ())), preferred_element_type=jnp.float32)
    grad_pooled = lax.dot_general(grad_rows, proj_weight, (((1,), (1,)), ((), ())), preferred_element_type=jnp.float32)
    grad_act = jnp.broadcast_to((grad_pooled / POS)[:, None, :], (BATCH, POS, C_HEAD)).reshape(BATCH * POS, C_HEAD)
    sig = jax.nn.sigmoid(pre)
    grad_pre = (grad_act * sig * (1.0 + pre * (1.0 - sig))).astype(jnp.bfloat16)
    grad_shift = lax.optimization_barrier(jnp.sum(grad_pre.astype(jnp.float32), axis=0))
    grad_head = lax.dot_general(feature_map, grad_pre, (((0,), (0,)), ((), ())), preferred_element_type=jnp.float32)
    return (loss, grad_head, grad_shift, grad_proj)
```

```python
import jax
import jax.numpy as jnp
from jax import lax
from jax.sharding import PartitionSpec as P

POS = 16
FULL_KERNEL_MAX_BATCH = 2048


def exchange_steps(mesh):
    steps = []
    for ax in ("dp", "blk"):
        size = mesh.shape[ax]
        if size & (size - 1):
            return []
        mask = 1
        while mask < size:
            steps.append((ax, mask))
            mask *= 2
    return steps


def swap(x, mesh, ax, mask):
    return lax.ppermute(x, ax, [(i, i ^ mask) for i in range(mesh.shape[ax])])


def my_bit(ax, mask):
    return (lax.axis_index(ax) & mask) != 0


def gather_blocks(zed, mesh, steps):
    order = list(reversed(steps))
    buf = zed[None]
    for ax, mask in order:
        got = swap(buf, mesh, ax, mask)
        buf = jnp.where(my_bit(ax, mask), jnp.stack([got, buf]), jnp.stack([buf, got]))
    block = sum(my_bit(ax, mask).astype(jnp.int32) << k for k, (ax, mask) in enumerate(order))
    return buf.reshape(-1, zed.shape[-1]), block


def halving_plan(shape, steps):
    plan, dims = [], list(shape)
    for _ in steps:
        if len(dims) == 2 and dims[0] % 16 == 0:
            plan.append(0)
            dims[0] //= 2
        elif len(dims) == 2 and dims[1] % 256 == 0:
            plan.append(1)
            dims[1] //= 2
        else:
            plan.append(None)
    return plan


def all_reduce(arrays, mesh, steps):
    plans = [halving_plan(a.shape, steps) for a in arrays]
    cur = list(arrays)
    for k, (ax, mask) in enumerate(steps):
        bit = my_bit(ax, mask).astype(jnp.int32)
        keeps, sends = [], []
        for a, plan in zip(cur, plans):
            d = plan[k]
            if d is None:
                keeps.append(a)
                sends.append(a)
            else:
                h = a.shape[d] // 2
                keeps.append(lax.dynamic_slice_in_dim(a, bit * h, h, axis=d))
                sends.append(lax.dynamic_slice_in_dim(a, (1 - bit) * h, h, axis=d))
        got = swap(sends, mesh, ax, mask)
        cur = [kk + g for kk, g in zip(keeps, got)]
    for k in reversed(range(len(steps))):
        ax, mask = steps[k]
        idx = [j for j, plan in enumerate(plans) if plans[j][k] is not None]
        if not idx:
            continue
        got = swap([cur[j] for j in idx], mesh, ax, mask)
        bit = my_bit(ax, mask)
        for j, g in zip(idx, got):
            d = plans[j][k]
            c = cur[j]
            cur[j] = jnp.where(bit, jnp.concatenate([g, c], axis=d), jnp.concatenate([c, g], axis=d))
    return cur


def pair_terms(rows_z, row_ids, piece, col_ids):
    sim = lax.dot_general(
        rows_z, piece, (((1,), (1,)), ((), ())), preferred_element_type=jnp.float32
    )
    kern = jnp.exp(4.0 * (sim - 1.0))
    kern = jnp.where(row_ids[:, None] == col_ids[None, :], jnp.float32(0.0), kern)
    return kern


def make_body(mesh):
    steps = exchange_steps(mesh)

    def body(feature_map, head_weight, head_shift, proj_weight):
        images = feature_map.shape[0] // POS
        channels = head_weight.shape[1]
        pre = jnp.dot(feature_map, head_weight, preferred_element_type=jnp.float32) + head_shift
        act = jax.nn.silu(pre)
        pooled = jnp.mean(act.reshape(images, POS, channels), axis=1).astype(jnp.bfloat16)
        proj = jnp.dot(pooled, proj_weight, preferred_element_type=jnp.float32)
        rnorm = jnp.sqrt(jnp.sum(proj * proj, axis=1, keepdims=True) + 1e-06)
        unit = proj / rnorm
        zed = unit.astype(jnp.bfloat16)
        batch = images * mesh.shape["blk"] * mesh.shape["dp"]
        if steps:
            piece, block = gather_blocks(zed, mesh, steps)
        else:
            piece = lax.all_gather(zed, ("blk", "dp"), axis=0, tiled=True)
            block = lax.axis_index(("blk", "dp"))
        my_ids = block * images + jnp.arange(images, dtype=jnp.int32)
        col_ids = jnp.arange(piece.shape[0], dtype=jnp.int32)
        kern = pair_terms(zed, my_ids, piece, col_ids)
        numer = jnp.dot(kern.astype(jnp.bfloat16), piece, preferred_element_type=jnp.float32)
        if batch <= FULL_KERNEL_MAX_BATCH:
            total = jnp.sum(pair_terms(piece, col_ids, piece, col_ids))
        else:
            total = lax.psum(jnp.sum(kern), ("blk", "dp"))
        loss = jnp.log(total / (batch * (batch - 1.0)))
        grad_unit = batch * 8.0 / total * numer
        grad_rows = (
            (grad_unit - unit * jnp.sum(unit * grad_unit, axis=1, keepdims=True)) / rnorm
        ).astype(jnp.bfloat16)
        grad_proj = lax.dot_general(
            pooled, grad_rows, (((0,), (0,)), ((), ())), preferred_element_type=jnp.float32
        )
        grad_pooled = lax.dot_general(
            grad_rows, proj_weight, (((1,), (1,)), ((), ())), preferred_element_type=jnp.float32
        )
        grad_act = jnp.broadcast_to(
            (grad_pooled / POS)[:, None, :], (images, POS, channels)
        ).reshape(images * POS, channels)
        sig = jax.nn.sigmoid(pre)
        grad_pre = (grad_act * sig * (1.0 + pre * (1.0 - sig))).astype(jnp.bfloat16)
        grad_shift = jnp.sum(grad_pre.astype(jnp.float32), axis=0)
        grad_head = lax.dot_general(
            feature_map, grad_pre, (((0,), (0,)), ((), ())), preferred_element_type=jnp.float32
        )
        if steps:
            grad_head, grad_proj, grad_shift = all_reduce([grad_head, grad_proj, grad_shift], mesh, steps)
        else:
            grad_head, grad_shift, grad_proj = lax.psum((grad_head, grad_shift, grad_proj), ("blk", "dp"))
        return (loss, grad_head, grad_shift, grad_proj)

    return body


def solution(mesh):
    return jax.shard_map(
        make_body(mesh),
        mesh=mesh,
        in_specs=(P(("blk", "dp"), None), P(), P(), P()),
        out_specs=(P(), P(), P(), P()),
        check_vma=False,
    )
```

```python
import jax
import jax.numpy as jnp
from jax import lax
from jax.sharding import PartitionSpec as P

POS = 16
FULL_KERNEL_MAX_BATCH = 2048


def exchange_steps(mesh):
    steps = []
    for ax in ("dp", "blk"):
        size = mesh.shape[ax]
        if size & (size - 1):
            return []
        mask = 1
        while mask < size:
            steps.append((ax, mask))
            mask *= 2
    return steps


def swap(x, mesh, ax, mask):
    return lax.ppermute(x, ax, [(i, i ^ mask) for i in range(mesh.shape[ax])])


def my_bit(ax, mask):
    return (lax.axis_index(ax) & mask) != 0


def gather_blocks(zed, mesh, steps):
    order = list(reversed(steps))
    buf = zed[None]
    for ax, mask in order:
        got = swap(buf, mesh, ax, mask)
        buf = jnp.where(my_bit(ax, mask), jnp.stack([got, buf]), jnp.stack([buf, got]))
    block = sum(my_bit(ax, mask).astype(jnp.int32) << k for k, (ax, mask) in enumerate(order))
    return buf.reshape(-1, zed.shape[-1]), block


def halving_plan(shape, steps):
    plan, dims = [], list(shape)
    for _ in steps:
        if len(dims) == 2 and dims[0] % 16 == 0:
            plan.append(0)
            dims[0] //= 2
        elif len(dims) == 2 and dims[1] % 256 == 0:
            plan.append(1)
            dims[1] //= 2
        else:
            plan.append(None)
    return plan


def all_reduce(arrays, mesh, steps):
    plans = [halving_plan(a.shape, steps) for a in arrays]
    cur = list(arrays)
    for k, (ax, mask) in enumerate(steps):
        bit = my_bit(ax, mask).astype(jnp.int32)
        keeps, sends = [], []
        for a, plan in zip(cur, plans):
            d = plan[k]
            if d is None:
                keeps.append(a)
                sends.append(a)
            else:
                h = a.shape[d] // 2
                keeps.append(lax.dynamic_slice_in_dim(a, bit * h, h, axis=d))
                sends.append(lax.dynamic_slice_in_dim(a, (1 - bit) * h, h, axis=d))
        got = swap(sends, mesh, ax, mask)
        cur = [kk + g for kk, g in zip(keeps, got)]
    for k in reversed(range(len(steps))):
        ax, mask = steps[k]
        idx = [j for j, plan in enumerate(plans) if plans[j][k] is not None]
        if not idx:
            continue
        got = swap([cur[j] for j in idx], mesh, ax, mask)
        bit = my_bit(ax, mask)
        for j, g in zip(idx, got):
            d = plans[j][k]
            c = cur[j]
            cur[j] = jnp.where(bit, jnp.concatenate([g, c], axis=d), jnp.concatenate([c, g], axis=d))
    return cur


def pair_terms(rows_z, row_ids, piece, col_ids):
    sim = lax.dot_general(
        rows_z, piece, (((1,), (1,)), ((), ())), preferred_element_type=jnp.float32
    )
    kern = jnp.exp(4.0 * (sim - 1.0))
    kern = jnp.where(row_ids[:, None] == col_ids[None, :], jnp.float32(0.0), kern)
    return kern


def make_body(mesh):
    steps = exchange_steps(mesh)

    def body(feature_map, head_weight, head_shift, proj_weight):
        images = feature_map.shape[0] // POS
        channels = head_weight.shape[1]
        pre = jnp.dot(feature_map, head_weight, preferred_element_type=jnp.float32) + head_shift
        act = jax.nn.silu(pre)
        pooled = jnp.mean(act.reshape(images, POS, channels), axis=1).astype(jnp.bfloat16)
        proj = jnp.dot(pooled, proj_weight, preferred_element_type=jnp.float32)
        rnorm = jnp.sqrt(jnp.sum(proj * proj, axis=1, keepdims=True) + 1e-06)
        unit = proj / rnorm
        zed = unit.astype(jnp.bfloat16)
        batch = images * mesh.shape["blk"] * mesh.shape["dp"]
        if steps:
            piece, block = gather_blocks(zed, mesh, steps)
        else:
            piece = lax.all_gather(zed, ("blk", "dp"), axis=0, tiled=True)
            block = lax.axis_index(("blk", "dp"))
        my_ids = block * images + jnp.arange(images, dtype=jnp.int32)
        col_ids = jnp.arange(piece.shape[0], dtype=jnp.int32)
        kern = pair_terms(zed, my_ids, piece, col_ids)
        numer = jnp.dot(kern.astype(jnp.bfloat16), piece, preferred_element_type=jnp.float32)
        if batch <= FULL_KERNEL_MAX_BATCH:
            total = jnp.sum(pair_terms(piece, col_ids, piece, col_ids))
        else:
            total = lax.psum(jnp.sum(kern), ("blk", "dp"))
        loss = jnp.log(total / (batch * (batch - 1.0)))
        grad_unit = batch * 8.0 / total * numer
        grad_rows = (
            (grad_unit - unit * jnp.sum(unit * grad_unit, axis=1, keepdims=True)) / rnorm
        ).astype(jnp.bfloat16)
        grad_pooled = lax.dot_general(
            grad_rows, proj_weight, (((1,), (1,)), ((), ())), preferred_element_type=jnp.float32
        )
        grad_act = jnp.broadcast_to(
            (grad_pooled / POS)[:, None, :], (images, POS, channels)
        ).reshape(images * POS, channels)
        sig = jax.nn.sigmoid(pre)
        grad_pre = (grad_act * sig * (1.0 + pre * (1.0 - sig))).astype(jnp.bfloat16)
        c_in = feature_map.shape[1]
        if steps:
            ones = jnp.ones((feature_map.shape[0], 1), feature_map.dtype)
            head_shift = lax.dot_general(
                jnp.concatenate([feature_map, ones], axis=1), grad_pre, (((0,), (0,)), ((), ())),
                preferred_element_type=jnp.float32,
            )
            proj_t = lax.dot_general(
                grad_rows, pooled, (((0,), (0,)), ((), ())), preferred_element_type=jnp.float32
            )
            used = head_shift.shape[0] + proj_t.shape[0]
            rows = -(-used // 64) * 64
            pad = jnp.zeros((rows - used, channels), jnp.float32)
            (buf,) = all_reduce([jnp.concatenate([head_shift, proj_t, pad], axis=0)], mesh, steps)
            grad_head = buf[:c_in]
            grad_shift = buf[c_in]
            grad_proj = buf[c_in + 1 : used].T
        else:
            grad_proj = lax.dot_general(
                pooled, grad_rows, (((0,), (0,)), ((), ())), preferred_element_type=jnp.float32
            )
            grad_shift = jnp.sum(grad_pre.astype(jnp.float32), axis=0)
            grad_head = lax.dot_general(
                feature_map, grad_pre, (((0,), (0,)), ((), ())), preferred_element_type=jnp.float32
            )
            grad_head, grad_shift, grad_proj = lax.psum((grad_head, grad_shift, grad_proj), ("blk", "dp"))
        return (loss, grad_head, grad_shift, grad_proj)

    return body


def solution(mesh):
    return jax.shard_map(
        make_body(mesh),
        mesh=mesh,
        in_specs=(P(("blk", "dp"), None), P(), P(), P()),
        out_specs=(P(), P(), P(), P()),
        check_vma=False,
    )
```

```python
import jax
import jax.numpy as jnp
from jax import lax
from jax.sharding import PartitionSpec as P

POS = 16
FULL_KERNEL_MAX_BATCH = 2048


def exchange_steps(mesh):
    steps = []
    for ax in ("dp", "blk"):
        size = mesh.shape[ax]
        if size & (size - 1):
            return []
        mask = 1
        while mask < size:
            steps.append((ax, mask))
            mask *= 2
    return steps


def swap(x, mesh, ax, mask):
    return lax.ppermute(x, ax, [(i, i ^ mask) for i in range(mesh.shape[ax])])


def my_bit(ax, mask):
    return (lax.axis_index(ax) & mask) != 0


def gather_blocks(zed, mesh, steps):
    order = list(reversed(steps))
    buf = zed[None]
    for ax, mask in order:
        got = swap(buf, mesh, ax, mask)
        buf = jnp.where(my_bit(ax, mask), jnp.stack([got, buf]), jnp.stack([buf, got]))
    block = sum(my_bit(ax, mask).astype(jnp.int32) << k for k, (ax, mask) in enumerate(order))
    return buf.reshape(-1, zed.shape[-1]), block


def halving_plan(shape, steps):
    plan, dims = [], list(shape)
    for _ in steps:
        if dims[0] % 16 == 0:
            plan.append(0)
            dims[0] //= 2
        elif dims[1] % 2 == 0 and dims[1] >= 256:
            plan.append(1)
            dims[1] //= 2
        else:
            plan.append(None)
    return plan


def all_reduce(colors, extra, mesh):
    plans = [halving_plan(a.shape, st) for a, st in colors]
    cur = [a for a, _ in colors]
    for k in range(len(colors[0][1])):
        sends, keeps = [], []
        for j, (_, st) in enumerate(colors):
            ax, mask = st[k]
            bit = my_bit(ax, mask).astype(jnp.int32)
            a, d = cur[j], plans[j][k]
            if d is None:
                keep = send = a
            else:
                h = a.shape[d] // 2
                keep = lax.dynamic_slice_in_dim(a, bit * h, h, axis=d)
                send = lax.dynamic_slice_in_dim(a, (1 - bit) * h, h, axis=d)
            if j == 0 and extra.size % send.shape[1] == 0:
                send = jnp.concatenate([send, extra.reshape(-1, send.shape[1])], axis=0)
            elif j == 0:
                extra = extra + swap(extra, mesh, ax, mask)
            keeps.append(keep)
            sends.append(send)
        for j, (_, st) in enumerate(colors):
            ax, mask = st[k]
            got = swap(sends[j], mesh, ax, mask)
            if j == 0 and got.shape[0] > keeps[0].shape[0]:
                rows = keeps[0].shape[0]
                extra = extra + got[rows:].reshape(extra.shape)
                got = got[:rows]
            cur[j] = keeps[j] + got
    for k in reversed(range(len(colors[0][1]))):
        for j, (_, st) in enumerate(colors):
            d = plans[j][k]
            if d is None:
                continue
            ax, mask = st[k]
            c = cur[j]
            g = swap(c, mesh, ax, mask)
            cur[j] = jnp.where(my_bit(ax, mask), jnp.concatenate([g, c], axis=d), jnp.concatenate([c, g], axis=d))
    return cur, extra


def color_orders(steps):
    if len(steps) < 4:
        return steps, steps
    middle = steps[1:-1]
    return steps, [steps[0]] + middle[1:] + middle[:1] + [steps[-1]]


def pair_terms(rows_z, row_ids, piece, col_ids):
    sim = lax.dot_general(
        rows_z, piece, (((1,), (1,)), ((), ())), preferred_element_type=jnp.float32
    )
    kern = jnp.exp(4.0 * (sim - 1.0))
    kern = jnp.where(row_ids[:, None] == col_ids[None, :], jnp.float32(0.0), kern)
    return kern


def make_body(mesh):
    steps = exchange_steps(mesh)

    def body(feature_map, head_weight, head_shift, proj_weight):
        images = feature_map.shape[0] // POS
        channels = head_weight.shape[1]
        pre = jnp.dot(feature_map, head_weight, preferred_element_type=jnp.float32) + head_shift
        act = jax.nn.silu(pre)
        pooled = jnp.mean(act.reshape(images, POS, channels), axis=1).astype(jnp.bfloat16)
        proj = jnp.dot(pooled, proj_weight, preferred_element_type=jnp.float32)
        rnorm = jnp.sqrt(jnp.sum(proj * proj, axis=1, keepdims=True) + 1e-06)
        unit = proj / rnorm
        zed = unit.astype(jnp.bfloat16)
        batch = images * mesh.shape["blk"] * mesh.shape["dp"]
        if steps:
            piece, block = gather_blocks(zed, mesh, steps)
        else:
            piece = lax.all_gather(zed, ("blk", "dp"), axis=0, tiled=True)
            block = lax.axis_index(("blk", "dp"))
        my_ids = block * images + jnp.arange(images, dtype=jnp.int32)
        col_ids = jnp.arange(piece.shape[0], dtype=jnp.int32)
        kern = pair_terms(zed, my_ids, piece, col_ids)
        numer = jnp.dot(kern.astype(jnp.bfloat16), piece, preferred_element_type=jnp.float32)
        if batch <= FULL_KERNEL_MAX_BATCH:
            total = jnp.sum(pair_terms(piece, col_ids, piece, col_ids))
        else:
            total = lax.psum(jnp.sum(kern), ("blk", "dp"))
        loss = jnp.log(total / (batch * (batch - 1.0)))
        grad_unit = batch * 8.0 / total * numer
        grad_rows = (
            (grad_unit - unit * jnp.sum(unit * grad_unit, axis=1, keepdims=True)) / rnorm
        ).astype(jnp.bfloat16)
        grad_pooled = lax.dot_general(
            grad_rows, proj_weight, (((1,), (1,)), ((), ())), preferred_element_type=jnp.float32
        )
        grad_act = jnp.broadcast_to(
            (grad_pooled / POS)[:, None, :], (images, POS, channels)
        ).reshape(images * POS, channels)
        sig = jax.nn.sigmoid(pre)
        grad_pre = (grad_act * sig * (1.0 + pre * (1.0 - sig))).astype(jnp.bfloat16)
        c_in = feature_map.shape[1]
        if steps:
            grad_proj = lax.dot_general(
                pooled, grad_rows, (((0,), (0,)), ((), ())), preferred_element_type=jnp.float32
            )
            grad_shift = jnp.sum(grad_pre.astype(jnp.float32), axis=0)
            grad_head = lax.dot_general(
                feature_map, grad_pre, (((0,), (0,)), ((), ())), preferred_element_type=jnp.float32
            )
            first, second = color_orders(steps)
            (grad_head, grad_proj), grad_shift = all_reduce(
                [(grad_head, first), (grad_proj, second)], grad_shift, mesh
            )
        else:
            grad_proj = lax.dot_general(
                pooled, grad_rows, (((0,), (0,)), ((), ())), preferred_element_type=jnp.float32
            )
            grad_shift = jnp.sum(grad_pre.astype(jnp.float32), axis=0)
            grad_head = lax.dot_general(
                feature_map, grad_pre, (((0,), (0,)), ((), ())), preferred_element_type=jnp.float32
            )
            grad_head, grad_shift, grad_proj = lax.psum((grad_head, grad_shift, grad_proj), ("blk", "dp"))
        return (loss, grad_head, grad_shift, grad_proj)

    return body


def solution(mesh):
    return jax.shard_map(
        make_body(mesh),
        mesh=mesh,
        in_specs=(P(("blk", "dp"), None), P(), P(), P()),
        out_specs=(P(), P(), P(), P()),
        check_vma=False,
    )
```

```python
import jax
import jax.numpy as jnp
from jax import lax
from jax.sharding import PartitionSpec as P

POS = 16
FULL_KERNEL_MAX_BATCH = 2048


def exchange_steps(mesh):
    steps = []
    for ax in ("dp", "blk"):
        size = mesh.shape[ax]
        if size & (size - 1):
            return []
        mask = 1
        while mask < size:
            steps.append((ax, mask))
            mask *= 2
    return steps


def swap(x, mesh, ax, mask):
    return lax.ppermute(x, ax, [(i, i ^ mask) for i in range(mesh.shape[ax])])


def my_bit(ax, mask):
    return (lax.axis_index(ax) & mask) != 0


def gather_blocks(zed, mesh, steps):
    order = list(reversed(steps))
    buf = zed[None]
    for ax, mask in order:
        got = swap(buf, mesh, ax, mask)
        buf = jnp.where(my_bit(ax, mask), jnp.stack([got, buf]), jnp.stack([buf, got]))
    block = sum(my_bit(ax, mask).astype(jnp.int32) << k for k, (ax, mask) in enumerate(order))
    return buf.reshape(-1, zed.shape[-1]), block


def halving_plan(shape, steps):
    plan, dims = [], list(shape)
    for _ in steps:
        if dims[0] % 16 == 0:
            plan.append(0)
            dims[0] //= 2
        elif dims[1] % 2 == 0 and dims[1] >= 256:
            plan.append(1)
            dims[1] //= 2
        else:
            plan.append(None)
    return plan


def combined_masks(steps, dp_size):
    masks = [mask if ax == "dp" else mask * dp_size for ax, mask in steps]
    if len(masks) < 4:
        return masks, masks
    middle = masks[1:-1]
    return masks, [masks[0]] + middle[1:] + middle[:1] + [masks[-1]]


def packed_all_reduce(buf, mesh, steps):
    axes = ("blk", "dp")
    n = mesh.shape["blk"] * mesh.shape["dp"]
    first, second = combined_masks(steps, mesh.shape["dp"])
    me = lax.axis_index(axes)
    group = (me & first[0]) != 0
    plan = halving_plan(buf.shape, steps)

    def partner_perm(k):
        return [(i, i ^ (second[k] if i & first[0] else first[k])) for i in range(n)]

    def bit_of(k):
        return (me & jnp.where(group, second[k], first[k])) != 0

    cur = buf
    for k in range(len(steps)):
        d = plan[k]
        bit = bit_of(k).astype(jnp.int32)
        if d is None:
            keep = send = cur
        else:
            h = cur.shape[d] // 2
            keep = lax.dynamic_slice_in_dim(cur, bit * h, h, axis=d)
            send = lax.dynamic_slice_in_dim(cur, (1 - bit) * h, h, axis=d)
        cur = keep + lax.ppermute(send, axes, partner_perm(k))
    for k in reversed(range(len(steps))):
        d = plan[k]
        if d is None:
            continue
        g = lax.ppermute(cur, axes, partner_perm(k))
        cur = jnp.where(bit_of(k), jnp.concatenate([g, cur], axis=d), jnp.concatenate([cur, g], axis=d))
    return cur


def pair_terms(rows_z, row_ids, piece, col_ids):
    sim = lax.dot_general(
        rows_z, piece, (((1,), (1,)), ((), ())), preferred_element_type=jnp.float32
    )
    kern = jnp.exp(4.0 * (sim - 1.0))
    kern = jnp.where(row_ids[:, None] == col_ids[None, :], jnp.float32(0.0), kern)
    return kern


def make_body(mesh):
    steps = exchange_steps(mesh)

    def body(feature_map, head_weight, head_shift, proj_weight):
        images = feature_map.shape[0] // POS
        channels = head_weight.shape[1]
        pre = jnp.dot(feature_map, head_weight, preferred_element_type=jnp.float32) + head_shift
        act = jax.nn.silu(pre)
        pooled = jnp.mean(act.reshape(images, POS, channels), axis=1).astype(jnp.bfloat16)
        proj = jnp.dot(pooled, proj_weight, preferred_element_type=jnp.float32)
        rnorm = jnp.sqrt(jnp.sum(proj * proj, axis=1, keepdims=True) + 1e-06)
        unit = proj / rnorm
        zed = unit.astype(jnp.bfloat16)
        batch = images * mesh.shape["blk"] * mesh.shape["dp"]
        if steps:
            piece, block = gather_blocks(zed, mesh, steps)
        else:
            piece = lax.all_gather(zed, ("blk", "dp"), axis=0, tiled=True)
            block = lax.axis_index(("blk", "dp"))
        my_ids = block * images + jnp.arange(images, dtype=jnp.int32)
        col_ids = jnp.arange(piece.shape[0], dtype=jnp.int32)
        kern = pair_terms(zed, my_ids, piece, col_ids)
        numer = jnp.dot(kern.astype(jnp.bfloat16), piece, preferred_element_type=jnp.float32)
        if batch <= FULL_KERNEL_MAX_BATCH:
            total = jnp.sum(pair_terms(piece, col_ids, piece, col_ids))
        else:
            total = lax.psum(jnp.sum(kern), ("blk", "dp"))
        loss = jnp.log(total / (batch * (batch - 1.0)))
        grad_unit = batch * 8.0 / total * numer
        grad_rows = (
            (grad_unit - unit * jnp.sum(unit * grad_unit, axis=1, keepdims=True)) / rnorm
        ).astype(jnp.bfloat16)
        grad_pooled = lax.dot_general(
            grad_rows, proj_weight, (((1,), (1,)), ((), ())), preferred_element_type=jnp.float32
        )
        grad_act = jnp.broadcast_to(
            (grad_pooled / POS)[:, None, :], (images, POS, channels)
        ).reshape(images * POS, channels)
        sig = jax.nn.sigmoid(pre)
        grad_pre = (grad_act * sig * (1.0 + pre * (1.0 - sig))).astype(jnp.bfloat16)
        c_in = feature_map.shape[1]
        if steps:
            grad_shift = jnp.sum(grad_pre.astype(jnp.float32), axis=0)
            grad_head = lax.dot_general(
                feature_map, grad_pre, (((0,), (0,)), ((), ())), preferred_element_type=jnp.float32
            )
            proj_t = lax.dot_general(
                grad_rows, pooled, (((0,), (0,)), ((), ())), preferred_element_type=jnp.float32
            )
            used = c_in + proj_t.shape[0] + 1
            rows = -(-used // 64) * 64
            packed = jnp.concatenate(
                [grad_head, proj_t, grad_shift[None], jnp.zeros((rows - used, channels), jnp.float32)], axis=0
            )
            packed = packed_all_reduce(packed, mesh, steps)
            grad_head = packed[:c_in]
            grad_proj = packed[c_in : used - 1].T
            grad_shift = packed[used - 1]
        else:
            grad_proj = lax.dot_general(
                pooled, grad_rows, (((0,), (0,)), ((), ())), preferred_element_type=jnp.float32
            )
            grad_shift = jnp.sum(grad_pre.astype(jnp.float32), axis=0)
            grad_head = lax.dot_general(
                feature_map, grad_pre, (((0,), (0,)), ((), ())), preferred_element_type=jnp.float32
            )
            grad_head, grad_shift, grad_proj = lax.psum((grad_head, grad_shift, grad_proj), ("blk", "dp"))
        return (loss, grad_head, grad_shift, grad_proj)

    return body


def solution(mesh):
    return jax.shard_map(
        make_body(mesh),
        mesh=mesh,
        in_specs=(P(("blk", "dp"), None), P(), P(), P()),
        out_specs=(P(), P(), P(), P()),
        check_vma=False,
    )
```

```python
import jax
import jax.numpy as jnp
from jax import lax
from jax.experimental import pallas as pl
from jax.sharding import PartitionSpec as P

POS = 16
FULL_KERNEL_MAX_BATCH = 2048


def exchange_steps(mesh):
    steps = []
    for ax in ("dp", "blk"):
        size = mesh.shape[ax]
        if size & (size - 1):
            return []
        mask = 1
        while mask < size:
            steps.append((ax, mask))
            mask *= 2
    return steps


def swap(x, mesh, ax, mask):
    return lax.ppermute(x, ax, [(i, i ^ mask) for i in range(mesh.shape[ax])])


def my_bit(ax, mask):
    return (lax.axis_index(ax) & mask) != 0


def gather_blocks(zed, mesh, steps):
    order = list(reversed(steps))
    buf = zed[None]
    for ax, mask in order:
        got = swap(buf, mesh, ax, mask)
        buf = jnp.where(my_bit(ax, mask), jnp.stack([got, buf]), jnp.stack([buf, got]))
    block = sum(my_bit(ax, mask).astype(jnp.int32) << k for k, (ax, mask) in enumerate(order))
    return buf.reshape(-1, zed.shape[-1]), block


def halving_plan(shape, steps):
    plan, dims = [], list(shape)
    for _ in steps:
        if dims[0] % 16 == 0:
            plan.append(0)
            dims[0] //= 2
        elif dims[1] % 2 == 0 and dims[1] >= 256:
            plan.append(1)
            dims[1] //= 2
        else:
            plan.append(None)
    return plan


def all_reduce(colors, extra, mesh):
    plans = [halving_plan(a.shape, st) for a, st in colors]
    cur = [a for a, _ in colors]
    for k in range(len(colors[0][1])):
        sends, keeps = [], []
        for j, (_, st) in enumerate(colors):
            ax, mask = st[k]
            bit = my_bit(ax, mask).astype(jnp.int32)
            a, d = cur[j], plans[j][k]
            if d is None:
                keep = send = a
            else:
                h = a.shape[d] // 2
                keep = lax.dynamic_slice_in_dim(a, bit * h, h, axis=d)
                send = lax.dynamic_slice_in_dim(a, (1 - bit) * h, h, axis=d)
            if j == 0 and extra.size % send.shape[1] == 0:
                send = jnp.concatenate([send, extra.reshape(-1, send.shape[1])], axis=0)
            elif j == 0:
                extra = extra + swap(extra, mesh, ax, mask)
            keeps.append(keep)
            sends.append(send)
        for j, (_, st) in enumerate(colors):
            ax, mask = st[k]
            got = swap(sends[j], mesh, ax, mask)
            if j == 0 and got.shape[0] > keeps[0].shape[0]:
                rows = keeps[0].shape[0]
                extra = extra + got[rows:].reshape(extra.shape)
                got = got[:rows]
            cur[j] = keeps[j] + got
    for k in reversed(range(len(colors[0][1]))):
        for j, (_, st) in enumerate(colors):
            d = plans[j][k]
            if d is None:
                continue
            ax, mask = st[k]
            c = cur[j]
            g = swap(c, mesh, ax, mask)
            cur[j] = jnp.where(my_bit(ax, mask), jnp.concatenate([g, c], axis=d), jnp.concatenate([c, g], axis=d))
    return cur, extra


def color_orders(steps):
    if len(steps) < 4:
        return steps, steps
    middle = steps[1:-1]
    return steps, [steps[0]] + middle[1:] + middle[:1] + [steps[-1]]


def pair_terms(rows_z, row_ids, piece, col_ids):
    sim = lax.dot_general(
        rows_z, piece, (((1,), (1,)), ((), ())), preferred_element_type=jnp.float32
    )
    kern = jnp.exp(4.0 * (sim - 1.0))
    kern = jnp.where(row_ids[:, None] == col_ids[None, :], jnp.float32(0.0), kern)
    return kern


def pooled_kernel(fm_ref, w_ref, shift_ref, out_ref):
    pre = jnp.dot(fm_ref[...], w_ref[...], preferred_element_type=jnp.float32) + shift_ref[...]
    act = pre * jax.nn.sigmoid(pre)
    images, channels = out_ref.shape
    out_ref[...] = jnp.mean(act.reshape(images, POS, channels), axis=1).astype(out_ref.dtype)


def pooled_of(feature_map, head_weight, head_shift, block_rows=128):
    rows, c_in = feature_map.shape
    channels = head_weight.shape[1]
    block_rows = block_rows if rows % block_rows == 0 else rows
    return pl.pallas_call(
        pooled_kernel,
        out_shape=jax.ShapeDtypeStruct((rows // POS, channels), jnp.bfloat16),
        grid=(rows // block_rows,),
        in_specs=[
            pl.BlockSpec((block_rows, c_in), lambda i: (i, 0)),
            pl.BlockSpec((c_in, channels), lambda i: (0, 0)),
            pl.BlockSpec((1, channels), lambda i: (0, 0)),
        ],
        out_specs=pl.BlockSpec((block_rows // POS, channels), lambda i: (i, 0)),
        cost_estimate=pl.CostEstimate(
            flops=2 * rows * c_in * channels,
            transcendentals=rows * channels,
            bytes_accessed=2 * (rows * c_in + c_in * channels + rows // POS * channels) + 4 * channels,
        ),
    )(feature_map, head_weight, head_shift.reshape(1, channels))


def make_body(mesh):
    steps = exchange_steps(mesh)

    def body(feature_map, head_weight, head_shift, proj_weight):
        images = feature_map.shape[0] // POS
        channels = head_weight.shape[1]
        pooled = pooled_of(feature_map, head_weight, head_shift)
        proj = jnp.dot(pooled, proj_weight, preferred_element_type=jnp.float32)
        rnorm = jnp.sqrt(jnp.sum(proj * proj, axis=1, keepdims=True) + 1e-06)
        unit = proj / rnorm
        zed = unit.astype(jnp.bfloat16)
        batch = images * mesh.shape["blk"] * mesh.shape["dp"]
        if steps:
            piece, block = gather_blocks(zed, mesh, steps)
        else:
            piece = lax.all_gather(zed, ("blk", "dp"), axis=0, tiled=True)
            block = lax.axis_index(("blk", "dp"))
        my_ids = block * images + jnp.arange(images, dtype=jnp.int32)
        col_ids = jnp.arange(piece.shape[0], dtype=jnp.int32)
        kern = pair_terms(zed, my_ids, piece, col_ids)
        numer = jnp.dot(kern.astype(jnp.bfloat16), piece, preferred_element_type=jnp.float32)
        if batch <= FULL_KERNEL_MAX_BATCH:
            total = jnp.sum(pair_terms(piece, col_ids, piece, col_ids))
        else:
            total = lax.psum(jnp.sum(kern), ("blk", "dp"))
        loss = jnp.log(total / (batch * (batch - 1.0)))
        grad_unit = batch * 8.0 / total * numer
        grad_rows = (
            (grad_unit - unit * jnp.sum(unit * grad_unit, axis=1, keepdims=True)) / rnorm
        ).astype(jnp.bfloat16)
        grad_pooled = lax.dot_general(
            grad_rows, proj_weight, (((1,), (1,)), ((), ())), preferred_element_type=jnp.float32
        )
        grad_act = jnp.broadcast_to(
            (grad_pooled / POS)[:, None, :], (images, POS, channels)
        ).reshape(images * POS, channels)
        pre = jnp.dot(feature_map, head_weight, preferred_element_type=jnp.float32) + head_shift
        sig = jax.nn.sigmoid(pre)
        grad_pre = (grad_act * sig * (1.0 + pre * (1.0 - sig))).astype(jnp.bfloat16)
        c_in = feature_map.shape[1]
        if steps:
            grad_proj = lax.dot_general(
                pooled, grad_rows, (((0,), (0,)), ((), ())), preferred_element_type=jnp.float32
            )
            grad_shift = jnp.sum(grad_pre.astype(jnp.float32), axis=0)
            grad_head = lax.dot_general(
                feature_map, grad_pre, (((0,), (0,)), ((), ())), preferred_element_type=jnp.float32
            )
            first, second = color_orders(steps)
            (grad_head, grad_proj), grad_shift = all_reduce(
                [(grad_head, first), (grad_proj, second)], grad_shift, mesh
            )
        else:
            grad_proj = lax.dot_general(
                pooled, grad_rows, (((0,), (0,)), ((), ())), preferred_element_type=jnp.float32
            )
            grad_shift = jnp.sum(grad_pre.astype(jnp.float32), axis=0)
            grad_head = lax.dot_general(
                feature_map, grad_pre, (((0,), (0,)), ((), ())), preferred_element_type=jnp.float32
            )
            grad_head, grad_shift, grad_proj = lax.psum((grad_head, grad_shift, grad_proj), ("blk", "dp"))
        return (loss, grad_head, grad_shift, grad_proj)

    return body


def solution(mesh):
    return jax.shard_map(
        make_body(mesh),
        mesh=mesh,
        in_specs=(P(("blk", "dp"), None), P(), P(), P()),
        out_specs=(P(), P(), P(), P()),
        check_vma=False,
    )
```

```python
import jax
import jax.numpy as jnp
from jax import lax
from jax.experimental import pallas as pl
from jax.sharding import PartitionSpec as P

POS = 16
FULL_KERNEL_MAX_BATCH = 2048


def exchange_steps(mesh):
    steps = []
    for ax in ("dp", "blk"):
        size = mesh.shape[ax]
        if size & (size - 1):
            return []
        mask = 1
        while mask < size:
            steps.append((ax, mask))
            mask *= 2
    return steps


def swap(x, mesh, ax, mask):
    return lax.ppermute(x, ax, [(i, i ^ mask) for i in range(mesh.shape[ax])])


def my_bit(ax, mask):
    return (lax.axis_index(ax) & mask) != 0


def gather_blocks(zed, mesh, steps):
    order = list(reversed(steps))
    buf = zed[None]
    for ax, mask in order:
        got = swap(buf, mesh, ax, mask)
        buf = jnp.where(my_bit(ax, mask), jnp.stack([got, buf]), jnp.stack([buf, got]))
    block = sum(my_bit(ax, mask).astype(jnp.int32) << k for k, (ax, mask) in enumerate(order))
    return buf.reshape(-1, zed.shape[-1]), block


def halving_plan(shape, steps):
    plan, dims = [], list(shape)
    for _ in steps:
        if dims[0] % 16 == 0:
            plan.append(0)
            dims[0] //= 2
        elif dims[1] % 2 == 0 and dims[1] >= 256:
            plan.append(1)
            dims[1] //= 2
        else:
            plan.append(None)
    return plan


def all_reduce(colors, extra, mesh):
    plans = [halving_plan(a.shape, st) for a, st in colors]
    cur = [a for a, _ in colors]
    for k in range(len(colors[0][1])):
        sends, keeps = [], []
        for j, (_, st) in enumerate(colors):
            ax, mask = st[k]
            bit = my_bit(ax, mask).astype(jnp.int32)
            a, d = cur[j], plans[j][k]
            if d is None:
                keep = send = a
            else:
                h = a.shape[d] // 2
                keep = lax.dynamic_slice_in_dim(a, bit * h, h, axis=d)
                send = lax.dynamic_slice_in_dim(a, (1 - bit) * h, h, axis=d)
            if j == 0 and extra.size % send.shape[1] == 0:
                send = jnp.concatenate([send, extra.reshape(-1, send.shape[1])], axis=0)
            elif j == 0:
                extra = extra + swap(extra, mesh, ax, mask)
            keeps.append(keep)
            sends.append(send)
        for j, (_, st) in enumerate(colors):
            ax, mask = st[k]
            got = swap(sends[j], mesh, ax, mask)
            if j == 0 and got.shape[0] > keeps[0].shape[0]:
                rows = keeps[0].shape[0]
                extra = extra + got[rows:].reshape(extra.shape)
                got = got[:rows]
            cur[j] = keeps[j] + got
    for k in reversed(range(len(colors[0][1]))):
        for j, (_, st) in enumerate(colors):
            d = plans[j][k]
            if d is None:
                continue
            ax, mask = st[k]
            c = cur[j]
            g = swap(c, mesh, ax, mask)
            cur[j] = jnp.where(my_bit(ax, mask), jnp.concatenate([g, c], axis=d), jnp.concatenate([c, g], axis=d))
    return cur, extra


def color_orders(steps):
    if len(steps) < 4:
        return steps, steps
    middle = steps[1:-1]
    return steps, [steps[0]] + middle[1:] + middle[:1] + [steps[-1]]


def pair_terms(rows_z, row_ids, piece, col_ids):
    sim = lax.dot_general(
        rows_z, piece, (((1,), (1,)), ((), ())), preferred_element_type=jnp.float32
    )
    kern = jnp.exp(4.0 * (sim - 1.0))
    kern = jnp.where(row_ids[:, None] == col_ids[None, :], jnp.float32(0.0), kern)
    return kern


def pooled_kernel(fm_t_ref, w_ref, shift_ref, out_ref):
    pre = lax.dot_general(
        fm_t_ref[...], w_ref[...], (((0,), (0,)), ((), ())), preferred_element_type=jnp.float32
    ) + shift_ref[...][None, :]
    act = pre * jax.nn.sigmoid(pre)
    images, channels = out_ref.shape
    out_ref[...] = jnp.mean(act.reshape(images, POS, channels), axis=1).astype(out_ref.dtype)


def pooled_of(feature_map, head_weight, head_shift, block_rows=128):
    rows, c_in = feature_map.shape
    channels = head_weight.shape[1]
    block_rows = block_rows if rows % block_rows == 0 else rows
    return pl.pallas_call(
        pooled_kernel,
        out_shape=jax.ShapeDtypeStruct((rows // POS, channels), jnp.bfloat16),
        grid=(rows // block_rows,),
        in_specs=[
            pl.BlockSpec((c_in, block_rows), lambda i: (0, i)),
            pl.BlockSpec((c_in, channels), lambda i: (0, 0)),
            pl.BlockSpec((channels,), lambda i: (0,)),
        ],
        out_specs=pl.BlockSpec((block_rows // POS, channels), lambda i: (i, 0)),
        cost_estimate=pl.CostEstimate(
            flops=2 * rows * c_in * channels,
            transcendentals=rows * channels,
            bytes_accessed=2 * (rows * c_in + c_in * channels + rows // POS * channels) + 4 * channels,
        ),
    )(feature_map.T, head_weight, head_shift)


def make_body(mesh):
    steps = exchange_steps(mesh)

    def body(feature_map, head_weight, head_shift, proj_weight):
        images = feature_map.shape[0] // POS
        channels = head_weight.shape[1]
        pooled = pooled_of(feature_map, head_weight, head_shift)
        proj = jnp.dot(pooled, proj_weight, preferred_element_type=jnp.float32)
        rnorm = jnp.sqrt(jnp.sum(proj * proj, axis=1, keepdims=True) + 1e-06)
        unit = proj / rnorm
        zed = unit.astype(jnp.bfloat16)
        batch = images * mesh.shape["blk"] * mesh.shape["dp"]
        if steps:
            piece, block = gather_blocks(zed, mesh, steps)
        else:
            piece = lax.all_gather(zed, ("blk", "dp"), axis=0, tiled=True)
            block = lax.axis_index(("blk", "dp"))
        my_ids = block * images + jnp.arange(images, dtype=jnp.int32)
        col_ids = jnp.arange(piece.shape[0], dtype=jnp.int32)
        kern = pair_terms(zed, my_ids, piece, col_ids)
        numer = jnp.dot(kern.astype(jnp.bfloat16), piece, preferred_element_type=jnp.float32)
        if batch <= FULL_KERNEL_MAX_BATCH:
            total = jnp.sum(pair_terms(piece, col_ids, piece, col_ids))
        else:
            total = lax.psum(jnp.sum(kern), ("blk", "dp"))
        loss = jnp.log(total / (batch * (batch - 1.0)))
        grad_unit = batch * 8.0 / total * numer
        grad_rows = (
            (grad_unit - unit * jnp.sum(unit * grad_unit, axis=1, keepdims=True)) / rnorm
        ).astype(jnp.bfloat16)
        grad_pooled = lax.dot_general(
            grad_rows, proj_weight, (((1,), (1,)), ((), ())), preferred_element_type=jnp.float32
        )
        grad_act = jnp.broadcast_to(
            (grad_pooled / POS)[:, None, :], (images, POS, channels)
        ).reshape(images * POS, channels)
        pre = jnp.dot(feature_map, head_weight, preferred_element_type=jnp.float32) + head_shift
        sig = jax.nn.sigmoid(pre)
        grad_pre = (grad_act * sig * (1.0 + pre * (1.0 - sig))).astype(jnp.bfloat16)
        c_in = feature_map.shape[1]
        if steps:
            grad_proj = lax.dot_general(
                pooled, grad_rows, (((0,), (0,)), ((), ())), preferred_element_type=jnp.float32
            )
            grad_shift = jnp.sum(grad_pre.astype(jnp.float32), axis=0)
            grad_head = lax.dot_general(
                feature_map, grad_pre, (((0,), (0,)), ((), ())), preferred_element_type=jnp.float32
            )
            first, second = color_orders(steps)
            (grad_head, grad_proj), grad_shift = all_reduce(
                [(grad_head, first), (grad_proj, second)], grad_shift, mesh
            )
        else:
            grad_proj = lax.dot_general(
                pooled, grad_rows, (((0,), (0,)), ((), ())), preferred_element_type=jnp.float32
            )
            grad_shift = jnp.sum(grad_pre.astype(jnp.float32), axis=0)
            grad_head = lax.dot_general(
                feature_map, grad_pre, (((0,), (0,)), ((), ())), preferred_element_type=jnp.float32
            )
            grad_head, grad_shift, grad_proj = lax.psum((grad_head, grad_shift, grad_proj), ("blk", "dp"))
        return (loss, grad_head, grad_shift, grad_proj)

    return body


def solution(mesh):
    return jax.shard_map(
        make_body(mesh),
        mesh=mesh,
        in_specs=(P(("blk", "dp"), None), P(), P(), P()),
        out_specs=(P(), P(), P(), P()),
        check_vma=False,
    )
```

```python
import jax
import jax.numpy as jnp
from jax import lax
from jax.experimental import pallas as pl
from jax.sharding import PartitionSpec as P

POS = 16
FULL_KERNEL_MAX_BATCH = 2048


def exchange_steps(mesh):
    steps = []
    for ax in ("dp", "blk"):
        size = mesh.shape[ax]
        if size & (size - 1):
            return []
        mask = 1
        while mask < size:
            steps.append((ax, mask))
            mask *= 2
    return steps


def swap(x, mesh, ax, mask):
    return lax.ppermute(x, ax, [(i, i ^ mask) for i in range(mesh.shape[ax])])


def my_bit(ax, mask):
    return (lax.axis_index(ax) & mask) != 0


def gather_blocks(zed, mesh, steps):
    order = list(reversed(steps))
    buf = zed[None]
    for ax, mask in order:
        got = swap(buf, mesh, ax, mask)
        buf = jnp.where(my_bit(ax, mask), jnp.stack([got, buf]), jnp.stack([buf, got]))
    block = sum(my_bit(ax, mask).astype(jnp.int32) << k for k, (ax, mask) in enumerate(order))
    return buf.reshape(-1, zed.shape[-1]), block


def halving_plan(shape, steps):
    plan, dims = [], list(shape)
    for _ in steps:
        if dims[0] % 16 == 0:
            plan.append(0)
            dims[0] //= 2
        elif dims[1] % 2 == 0 and dims[1] >= 256:
            plan.append(1)
            dims[1] //= 2
        else:
            plan.append(None)
    return plan


def all_reduce(colors, extra, mesh):
    plans = [halving_plan(a.shape, st) for a, st in colors]
    cur = [a for a, _ in colors]
    for k in range(len(colors[0][1])):
        sends, keeps = [], []
        for j, (_, st) in enumerate(colors):
            ax, mask = st[k]
            bit = my_bit(ax, mask).astype(jnp.int32)
            a, d = cur[j], plans[j][k]
            if d is None:
                keep = send = a
            else:
                h = a.shape[d] // 2
                keep = lax.dynamic_slice_in_dim(a, bit * h, h, axis=d)
                send = lax.dynamic_slice_in_dim(a, (1 - bit) * h, h, axis=d)
            if j == 0 and extra.size % send.shape[1] == 0:
                send = jnp.concatenate([send, extra.reshape(-1, send.shape[1])], axis=0)
            elif j == 0:
                extra = extra + swap(extra, mesh, ax, mask)
            keeps.append(keep)
            sends.append(send)
        for j, (_, st) in enumerate(colors):
            ax, mask = st[k]
            got = swap(sends[j], mesh, ax, mask)
            if j == 0 and got.shape[0] > keeps[0].shape[0]:
                rows = keeps[0].shape[0]
                extra = extra + got[rows:].reshape(extra.shape)
                got = got[:rows]
            cur[j] = keeps[j] + got
    for k in reversed(range(len(colors[0][1]))):
        for j, (_, st) in enumerate(colors):
            d = plans[j][k]
            if d is None:
                continue
            ax, mask = st[k]
            c = cur[j]
            g = swap(c, mesh, ax, mask)
            cur[j] = jnp.where(my_bit(ax, mask), jnp.concatenate([g, c], axis=d), jnp.concatenate([c, g], axis=d))
    return cur, extra


def color_orders(steps):
    if len(steps) < 4:
        return steps, steps
    middle = steps[1:-1]
    return steps, [steps[0]] + middle[1:] + middle[:1] + [steps[-1]]


def pair_terms(rows_z, row_ids, piece, col_ids):
    sim = lax.dot_general(
        rows_z, piece, (((1,), (1,)), ((), ())), preferred_element_type=jnp.float32
    )
    kern = jnp.exp(4.0 * (sim - 1.0))
    kern = jnp.where(row_ids[:, None] == col_ids[None, :], jnp.float32(0.0), kern)
    return kern


def pooled_kernel(fm_t_ref, w_ref, shift_ref, out_ref):
    pre = lax.dot_general(
        fm_t_ref[...], w_ref[...], (((0,), (0,)), ((), ())), preferred_element_type=jnp.float32
    ) + shift_ref[...][None, :]
    act = pre * jax.nn.sigmoid(pre)
    images, channels = out_ref.shape
    out_ref[...] = jnp.mean(act.reshape(images, POS, channels), axis=1).astype(out_ref.dtype)


def pooled_of(feature_map, head_weight, head_shift, block_rows=128):
    rows, c_in = feature_map.shape
    channels = head_weight.shape[1]
    block_rows = block_rows if rows % block_rows == 0 else rows
    return pl.pallas_call(
        pooled_kernel,
        out_shape=jax.ShapeDtypeStruct((rows // POS, channels), jnp.bfloat16),
        grid=(rows // block_rows,),
        in_specs=[
            pl.BlockSpec((c_in, block_rows), lambda i: (0, i)),
            pl.BlockSpec((c_in, channels), lambda i: (0, 0)),
            pl.BlockSpec((channels,), lambda i: (0,)),
        ],
        out_specs=pl.BlockSpec((block_rows // POS, channels), lambda i: (i, 0)),
        cost_estimate=pl.CostEstimate(
            flops=2 * rows * c_in * channels,
            transcendentals=rows * channels,
            bytes_accessed=2 * (rows * c_in + c_in * channels + rows // POS * channels) + 4 * channels,
        ),
    )(feature_map.T, head_weight, head_shift)


def make_body(mesh):
    steps = exchange_steps(mesh)

    def body(feature_map, head_weight, head_shift, proj_weight):
        images = feature_map.shape[0] // POS
        channels = head_weight.shape[1]
        pooled = pooled_of(feature_map, head_weight, head_shift)
        pre = jnp.dot(feature_map, head_weight, preferred_element_type=jnp.float32) + head_shift
        sig = jax.nn.sigmoid(pre)
        factor = lax.optimization_barrier(sig * (1.0 + pre * (1.0 - sig)))
        proj = jnp.dot(pooled, proj_weight, preferred_element_type=jnp.float32)
        rnorm = jnp.sqrt(jnp.sum(proj * proj, axis=1, keepdims=True) + 1e-06)
        unit = proj / rnorm
        zed = unit.astype(jnp.bfloat16)
        batch = images * mesh.shape["blk"] * mesh.shape["dp"]
        if steps:
            piece, block = gather_blocks(zed, mesh, steps)
        else:
            piece = lax.all_gather(zed, ("blk", "dp"), axis=0, tiled=True)
            block = lax.axis_index(("blk", "dp"))
        my_ids = block * images + jnp.arange(images, dtype=jnp.int32)
        col_ids = jnp.arange(piece.shape[0], dtype=jnp.int32)
        kern = pair_terms(zed, my_ids, piece, col_ids)
        numer = jnp.dot(kern.astype(jnp.bfloat16), piece, preferred_element_type=jnp.float32)
        if batch <= FULL_KERNEL_MAX_BATCH:
            total = jnp.sum(pair_terms(piece, col_ids, piece, col_ids))
        else:
            total = lax.psum(jnp.sum(kern), ("blk", "dp"))
        loss = jnp.log(total / (batch * (batch - 1.0)))
        grad_unit = batch * 8.0 / total * numer
        grad_rows = (
            (grad_unit - unit * jnp.sum(unit * grad_unit, axis=1, keepdims=True)) / rnorm
        ).astype(jnp.bfloat16)
        grad_pooled = lax.dot_general(
            grad_rows, proj_weight, (((1,), (1,)), ((), ())), preferred_element_type=jnp.float32
        )
        grad_act = jnp.broadcast_to(
            (grad_pooled / POS)[:, None, :], (images, POS, channels)
        ).reshape(images * POS, channels)
        grad_pre = (grad_act * factor).astype(jnp.bfloat16)
        c_in = feature_map.shape[1]
        if steps:
            grad_proj = lax.dot_general(
                pooled, grad_rows, (((0,), (0,)), ((), ())), preferred_element_type=jnp.float32
            )
            grad_shift = jnp.sum(grad_pre.astype(jnp.float32), axis=0)
            grad_head = lax.dot_general(
                feature_map, grad_pre, (((0,), (0,)), ((), ())), preferred_element_type=jnp.float32
            )
            first, second = color_orders(steps)
            (grad_head, grad_proj), grad_shift = all_reduce(
                [(grad_head, first), (grad_proj, second)], grad_shift, mesh
            )
        else:
            grad_proj = lax.dot_general(
                pooled, grad_rows, (((0,), (0,)), ((), ())), preferred_element_type=jnp.float32
            )
            grad_shift = jnp.sum(grad_pre.astype(jnp.float32), axis=0)
            grad_head = lax.dot_general(
                feature_map, grad_pre, (((0,), (0,)), ((), ())), preferred_element_type=jnp.float32
            )
            grad_head, grad_shift, grad_proj = lax.psum((grad_head, grad_shift, grad_proj), ("blk", "dp"))
        return (loss, grad_head, grad_shift, grad_proj)

    return body


def solution(mesh):
    return jax.shard_map(
        make_body(mesh),
        mesh=mesh,
        in_specs=(P(("blk", "dp"), None), P(), P(), P()),
        out_specs=(P(), P(), P(), P()),
        check_vma=False,
    )
```

```python
import jax
import jax.numpy as jnp
from jax import lax
from jax.experimental import pallas as pl
from jax.sharding import PartitionSpec as P

POS = 16
FULL_KERNEL_MAX_BATCH = 2048


def exchange_steps(mesh):
    steps = []
    for ax in ("dp", "blk"):
        size = mesh.shape[ax]
        if size & (size - 1):
            return []
        mask = 1
        while mask < size:
            steps.append((ax, mask))
            mask *= 2
    return steps


def swap(x, mesh, ax, mask):
    return lax.ppermute(x, ax, [(i, i ^ mask) for i in range(mesh.shape[ax])])


def my_bit(ax, mask):
    return (lax.axis_index(ax) & mask) != 0


def gather_blocks(zed, mesh, steps):
    order = list(reversed(steps))
    buf = zed[None]
    for ax, mask in order:
        got = swap(buf, mesh, ax, mask)
        buf = jnp.where(my_bit(ax, mask), jnp.stack([got, buf]), jnp.stack([buf, got]))
    block = sum(my_bit(ax, mask).astype(jnp.int32) << k for k, (ax, mask) in enumerate(order))
    return buf.reshape(-1, zed.shape[-1]), block


def halving_plan(shape, steps):
    plan, dims = [], list(shape)
    for _ in steps:
        if dims[0] % 16 == 0:
            plan.append(0)
            dims[0] //= 2
        elif dims[1] % 2 == 0 and dims[1] >= 256:
            plan.append(1)
            dims[1] //= 2
        else:
            plan.append(None)
    return plan


def all_reduce(colors, extra, mesh):
    plans = [halving_plan(a.shape, st) for a, st in colors]
    cur = [a for a, _ in colors]
    for k in range(len(colors[0][1])):
        sends, keeps = [], []
        for j, (_, st) in enumerate(colors):
            ax, mask = st[k]
            bit = my_bit(ax, mask).astype(jnp.int32)
            a, d = cur[j], plans[j][k]
            if d is None:
                keep = send = a
            else:
                h = a.shape[d] // 2
                keep = lax.dynamic_slice_in_dim(a, bit * h, h, axis=d)
                send = lax.dynamic_slice_in_dim(a, (1 - bit) * h, h, axis=d)
            if j == 0 and extra.size % send.shape[1] == 0:
                send = jnp.concatenate([send, extra.reshape(-1, send.shape[1])], axis=0)
            elif j == 0:
                extra = extra + swap(extra, mesh, ax, mask)
            keeps.append(keep)
            sends.append(send)
        for j, (_, st) in enumerate(colors):
            ax, mask = st[k]
            got = swap(sends[j], mesh, ax, mask)
            if j == 0 and got.shape[0] > keeps[0].shape[0]:
                rows = keeps[0].shape[0]
                extra = extra + got[rows:].reshape(extra.shape)
                got = got[:rows]
            cur[j] = keeps[j] + got
    for k in reversed(range(len(colors[0][1]))):
        for j, (_, st) in enumerate(colors):
            d = plans[j][k]
            if d is None:
                continue
            ax, mask = st[k]
            c = cur[j]
            g = swap(c, mesh, ax, mask)
            cur[j] = jnp.where(my_bit(ax, mask), jnp.concatenate([g, c], axis=d), jnp.concatenate([c, g], axis=d))
    return cur, extra


def color_orders(steps):
    if len(steps) < 4:
        return steps, steps
    middle = steps[1:-1]
    return steps, [steps[0]] + middle[1:] + middle[:1] + [steps[-1]]


def pair_terms(rows_z, row_ids, piece, col_ids):
    sim = lax.dot_general(
        rows_z, piece, (((1,), (1,)), ((), ())), preferred_element_type=jnp.float32
    )
    kern = jnp.exp(4.0 * (sim - 1.0))
    kern = jnp.where(row_ids[:, None] == col_ids[None, :], jnp.float32(0.0), kern)
    return kern


def pooled_kernel(fm_t_ref, w_ref, shift_ref, out_ref):
    pre = lax.dot_general(
        fm_t_ref[...], w_ref[...], (((0,), (0,)), ((), ())), preferred_element_type=jnp.float32
    ) + shift_ref[...][None, :]
    act = pre * jax.nn.sigmoid(pre)
    images, channels = out_ref.shape
    out_ref[...] = jnp.mean(act.reshape(images, POS, channels), axis=1).astype(out_ref.dtype)


def pooled_of(feature_map, head_weight, head_shift, block_rows=640):
    rows, c_in = feature_map.shape
    channels = head_weight.shape[1]
    block_rows = block_rows if rows % block_rows == 0 else rows
    return pl.pallas_call(
        pooled_kernel,
        out_shape=jax.ShapeDtypeStruct((rows // POS, channels), jnp.bfloat16),
        grid=(rows // block_rows,),
        in_specs=[
            pl.BlockSpec((c_in, block_rows), lambda i: (0, i)),
            pl.BlockSpec((c_in, channels), lambda i: (0, 0)),
            pl.BlockSpec((channels,), lambda i: (0,)),
        ],
        out_specs=pl.BlockSpec((block_rows // POS, channels), lambda i: (i, 0)),
        cost_estimate=pl.CostEstimate(
            flops=2 * rows * c_in * channels,
            transcendentals=rows * channels,
            bytes_accessed=2 * (rows * c_in + c_in * channels + rows // POS * channels) + 4 * channels,
        ),
    )(feature_map.T, head_weight, head_shift)


def make_body(mesh):
    steps = exchange_steps(mesh)

    def body(feature_map, head_weight, head_shift, proj_weight):
        images = feature_map.shape[0] // POS
        channels = head_weight.shape[1]
        pooled = pooled_of(feature_map, head_weight, head_shift)
        pre = jnp.dot(feature_map, head_weight, preferred_element_type=jnp.float32) + head_shift
        sig = jax.nn.sigmoid(pre)
        factor = lax.optimization_barrier(sig * (1.0 + pre * (1.0 - sig)))
        proj = jnp.dot(pooled, proj_weight, preferred_element_type=jnp.float32)
        rnorm = jnp.sqrt(jnp.sum(proj * proj, axis=1, keepdims=True) + 1e-06)
        unit = proj / rnorm
        zed = unit.astype(jnp.bfloat16)
        batch = images * mesh.shape["blk"] * mesh.shape["dp"]
        if steps:
            piece, block = gather_blocks(zed, mesh, steps)
        else:
            piece = lax.all_gather(zed, ("blk", "dp"), axis=0, tiled=True)
            block = lax.axis_index(("blk", "dp"))
        my_ids = block * images + jnp.arange(images, dtype=jnp.int32)
        col_ids = jnp.arange(piece.shape[0], dtype=jnp.int32)
        kern = pair_terms(zed, my_ids, piece, col_ids)
        numer = jnp.dot(kern.astype(jnp.bfloat16), piece, preferred_element_type=jnp.float32)
        if batch <= FULL_KERNEL_MAX_BATCH:
            total = jnp.sum(pair_terms(piece, col_ids, piece, col_ids))
        else:
            total = lax.psum(jnp.sum(kern), ("blk", "dp"))
        loss = jnp.log(total / (batch * (batch - 1.0)))
        grad_unit = batch * 8.0 / total * numer
        grad_rows = (
            (grad_unit - unit * jnp.sum(unit * grad_unit, axis=1, keepdims=True)) / rnorm
        ).astype(jnp.bfloat16)
        grad_pooled = lax.dot_general(
            grad_rows, proj_weight, (((1,), (1,)), ((), ())), preferred_element_type=jnp.float32
        )
        grad_act = jnp.broadcast_to(
            (grad_pooled / POS)[:, None, :], (images, POS, channels)
        ).reshape(images * POS, channels)
        grad_pre = (grad_act * factor).astype(jnp.bfloat16)
        c_in = feature_map.shape[1]
        if steps:
            grad_proj = lax.dot_general(
                pooled, grad_rows, (((0,), (0,)), ((), ())), preferred_element_type=jnp.float32
            )
            grad_shift = jnp.sum(grad_pre.astype(jnp.float32), axis=0)
            grad_head = lax.dot_general(
                feature_map, grad_pre, (((0,), (0,)), ((), ())), preferred_element_type=jnp.float32
            )
            first, second = color_orders(steps)
            (grad_head, grad_proj), grad_shift = all_reduce(
                [(grad_head, first), (grad_proj, second)], grad_shift, mesh
            )
        else:
            grad_proj = lax.dot_general(
                pooled, grad_rows, (((0,), (0,)), ((), ())), preferred_element_type=jnp.float32
            )
            grad_shift = jnp.sum(grad_pre.astype(jnp.float32), axis=0)
            grad_head = lax.dot_general(
                feature_map, grad_pre, (((0,), (0,)), ((), ())), preferred_element_type=jnp.float32
            )
            grad_head, grad_shift, grad_proj = lax.psum((grad_head, grad_shift, grad_proj), ("blk", "dp"))
        return (loss, grad_head, grad_shift, grad_proj)

    return body


def solution(mesh):
    return jax.shard_map(
        make_body(mesh),
        mesh=mesh,
        in_specs=(P(("blk", "dp"), None), P(), P(), P()),
        out_specs=(P(), P(), P(), P()),
        check_vma=False,
    )
```
